512 devices in a mesh: ctx: 32 (over y, x), fsdp: 16 (over z, core).
Axes of the slice: x: 4, y: 8, z: 8, core: 2. Of those that a mesh axis runs over, the one named last changes fastest.
Arguments:
- tokens: bfloat16 [131072, 4096], P(('ctx', 'fsdp')), may hold values from -48 to 48
- query_weight: bfloat16 [4096, 512], P('fsdp'), may hold values from -0.09375 to 0.09375
- key_weight: bfloat16 [4096, 128], P('fsdp'), may hold values from -0.09375 to 0.09375
- value_weight: bfloat16 [4096, 128], P('fsdp'), may hold values from -0.09375 to 0.09375
- chosen: int32 [256, 2], replicated, may hold values from 0 to 253, as said below
Outputs:
- attended: bfloat16 [131072, 512], P(('ctx', 'fsdp'))
The draws below stay inside these ranges and needn't reach their ends.
Inputs may be any that keep to these rules, and one draw needn't show every extreme that they name: `chosen`: for query block q >= 3 both entries are distinct and below q - 1; block 2 names block 0 twice; blocks 0 and 1 name 0 twice, which selects nothing. The last block always selects block 253.
All inputs are finite; a program needn't handle non-finite values.
Results may differ from the reference program's by a relative error of at most 0.0065.
The reference program's roundings to bfloat16 on the way (of `queries`, `keys`, `values` and `rounded`) count: a program that leaves them out, or rounds other values in their place, can miss the bound.
Values may be sent and summed in bfloat16 or wider, within the bound.
No kernel may reach another device: no remote copies, remote signals or barrier semaphores. Data moves between devices by JAX's collectives and lax.ppermute only.
A program may use at most 64 MiB of HBM per device.

```python
import jax
import jax.numpy as jnp
from jax import lax

D = 4096
HD = 128
QH = 4
BLOCK = 512
NBLK = 256
SEQ = 131072


def draw_tokens(key, part):
    first = jax.random.fold_in(key, 0)
    base = jax.random.truncated_normal(first, -4.5, 4.5, (SEQ, D), jnp.float32)
    return base.astype(jnp.bfloat16)


def draw_chosen(key, part):
    first, second = jax.random.split(jax.random.fold_in(key, 7))
    block = jnp.arange(NBLK, dtype=jnp.int32)
    primary = jax.random.randint(first, (NBLK,), 0, jnp.maximum(block - 1, 1))
    primary = jnp.where(block == NBLK - 1, NBLK - 3, primary)
    other = jax.random.randint(second, (NBLK,), 0, jnp.maximum(block - 2, 1))
    other = other + (other >= primary).astype(jnp.int32)
    other = jnp.where(block < 3, primary, other)
    return jnp.stack([primary, other], axis=1).astype(jnp.int32)


def levels(key, extent, shards, least, high):
    def one(axis_at, blocks):
        draws = jax.random.uniform(jax.random.fold_in(jax.random.fold_in(key, 6), axis_at), (blocks,), jnp.float32, least / len(shards), high / len(shards))
        return jnp.repeat(jnp.exp(draws), extent[axis_at] // blocks).reshape((-1,) + (1,) * (len(extent) - axis_at - 1))

    level = one(*shards[0])
    for cut in shards[1:]:
        level = level * one(*cut)
    return level


def centred(stream_key, shape, scale, limit, shards=(), held_as=jnp.bfloat16):
    values = jax.random.normal(stream_key, shape, jnp.float32) * scale
    if len(shards) > 0:
        values = levels(stream_key, shape, shards, -0.22, 0.18) * values
    return jnp.clip(values, min=-limit, max=limit).astype(held_as)


def setup_inputs(seed: int = 0) -> dict:
    streams_of = jax.random.split(jax.random.key(seed), 6)
    tokens = draw_tokens(jax.random.fold_in(streams_of[5], 71), 0)
    query_weight = centred(streams_of[1], (D, QH * HD), D ** -0.5, 0.09375, ((0, 16),))
    key_weight = centred(streams_of[2], (D, HD), D ** -0.5, 0.09375, ((0, 16),))
    value_weight = centred(streams_of[3], (D, HD), D ** -0.5, 0.09375, ((0, 16),))
    chosen = draw_chosen(jax.random.fold_in(streams_of[5], 71), 0)
    return {"tokens": tokens, "query_weight": query_weight, "key_weight": key_weight, "value_weight": value_weight, "chosen": chosen}


def reference(tokens, query_weight, key_weight, value_weight, chosen):
    queries = jnp.dot(tokens, query_weight, preferred_element_type=jnp.float32).astype(jnp.bfloat16)
    keys = jnp.dot(tokens, key_weight, preferred_element_type=jnp.float32).astype(jnp.bfloat16)
    values = jnp.dot(tokens, value_weight, preferred_element_type=jnp.float32).astype(jnp.bfloat16)
    scale = HD ** -0.5
    half_rows = BLOCK // 2

    def one_block(block_index):
        start = (block_index * BLOCK).astype(jnp.int32)
        before_start = jnp.maximum(start - half_rows, 0).astype(jnp.int32)
        query_rows = lax.dynamic_slice_in_dim(queries, start, BLOCK, 0).reshape(BLOCK, QH, HD)
        first_pick = chosen[block_index, 0]
        second_pick = chosen[block_index, 1]
        first_live = first_pick < block_index - 1
        second_live = (second_pick < block_index - 1) & (second_pick != first_pick)
        first_start = (first_pick * BLOCK).astype(jnp.int32)
        second_start = (second_pick * BLOCK).astype(jnp.int32)
        key_rows = jnp.concatenate([
            lax.dynamic_slice_in_dim(keys, before_start, half_rows, 0),
            lax.dynamic_slice_in_dim(keys, start, BLOCK, 0),
            lax.dynamic_slice_in_dim(keys, first_start, BLOCK, 0),
            lax.dynamic_slice_in_dim(keys, second_start, BLOCK, 0)], axis=0)
        value_rows = jnp.concatenate([
            lax.dynamic_slice_in_dim(values, before_start, half_rows, 0),
            lax.dynamic_slice_in_dim(values, start, BLOCK, 0),
            lax.dynamic_slice_in_dim(values, first_start, BLOCK, 0),
            lax.dynamic_slice_in_dim(values, second_start, BLOCK, 0)], axis=0)
        scores = jnp.einsum("qhd,kd->hqk", query_rows.astype(jnp.float32), key_rows.astype(jnp.float32)) * scale
        position = jnp.arange(BLOCK, dtype=jnp.int32)
        causal = position[None, :] <= position[:, None]
        before_seen = jnp.broadcast_to((position[:, None] < half_rows) & (block_index > 0), (BLOCK, half_rows))
        visible = jnp.concatenate([
            before_seen,
            causal,
            jnp.broadcast_to(first_live, (BLOCK, BLOCK)),
            jnp.broadcast_to(second_live, (BLOCK, BLOCK))], axis=1)
        scores = jnp.where(visible[None], scores, -jnp.inf)
        highest = jnp.max(scores, axis=2, keepdims=True)
        probs = jnp.exp(scores - highest)
        denominator = jnp.sum(probs, axis=2, keepdims=True)
        rounded = lax.optimization_barrier(probs.astype(jnp.bfloat16)).astype(jnp.float32)
        mixed = jnp.einsum("hqk,kd->hqd", rounded, value_rows.astype(jnp.float32)) / denominator
        return jnp.transpose(mixed, (1, 0, 2)).reshape(BLOCK, QH * HD).astype(jnp.bfloat16)

    blocks_out = lax.map(one_block, jnp.arange(NBLK, dtype=jnp.int32))
    return blocks_out.reshape(SEQ, QH * HD)
```

```python
import jax
import jax.numpy as jnp
from jax import lax
from jax.sharding import PartitionSpec as P

QH = 4


def from_behind(array, axis, by):
    peers = lax.axis_size(axis)
    pairs = [(i, i + by) for i in range(peers) if 0 <= i + by < peers]
    return lax.ppermute(array, axis, pairs)


def gather_rows(array, axis):
    peers = lax.axis_size(axis)
    spread = jnp.broadcast_to(array[None], (peers,) + array.shape)
    got = lax.all_to_all(spread, axis, split_axis=0, concat_axis=0, tiled=True)
    return got.reshape((peers * array.shape[0],) + array.shape[1:])


def swap_partner(array, axis):
    peers = lax.axis_size(axis)
    pairs = [(i, i ^ 1) for i in range(peers)]
    return lax.ppermute(array, axis, pairs)


def per_device(tokens, query_weight, key_weight, value_weight, chosen):
    token_rows = tokens.shape[0]
    head_width = key_weight.shape[1]
    lane_count = lax.axis_size("fsdp")
    lane_index = lax.axis_index("fsdp")
    group_index = lax.axis_index("ctx")
    blocks_group = lane_count // 2
    my_block = group_index * blocks_group + lane_index // 2
    global_index = group_index * lane_count + lane_index

    kv_weight = gather_rows(jnp.concatenate([key_weight, value_weight], axis=1), "fsdp")
    kv_f32 = jnp.dot(tokens, kv_weight, preferred_element_type=jnp.float32)
    key_value = kv_f32.astype(jnp.bfloat16)

    query_weight, key_value = lax.optimization_barrier((query_weight, key_value))

    candidates = lax.all_gather(key_value, "ctx", axis=0, tiled=True).reshape(
        -1, token_rows, 2 * head_width
    )
    before_pair = from_behind(key_value, ("ctx", "fsdp"), 1)
    own_block = jnp.concatenate([before_pair, key_value], axis=0)

    q_weight = gather_rows(query_weight, "fsdp")
    queries = jnp.dot(tokens, q_weight, preferred_element_type=jnp.float32)
    queries = queries.astype(jnp.bfloat16).reshape(token_rows, QH, head_width)

    queries, candidates = lax.optimization_barrier((queries, candidates))

    dest_block = group_index * blocks_group + jnp.arange(lane_count, dtype=jnp.int32) // 2
    dest_pick = chosen[dest_block, jnp.arange(lane_count, dtype=jnp.int32) % 2]
    outgoing = jnp.take(candidates, dest_pick // blocks_group, axis=0)
    incoming = lax.all_to_all(outgoing, "fsdp", split_axis=0, concat_axis=0, tiled=True)

    mine = lax.dynamic_index_in_dim(chosen, my_block, 0, keepdims=False)
    my_choice = lane_index % 2
    my_pick = jnp.where(my_choice == 0, mine[0], mine[1])
    place = my_pick % blocks_group * 2
    block_mine = lax.dynamic_slice_in_dim(incoming, place, 2, 0).reshape(
        2 * token_rows, 2 * head_width
    )
    block_partner = swap_partner(block_mine, "fsdp")

    key_rows = jnp.concatenate(
        [own_block[:, :head_width], block_mine[:, :head_width], block_partner[:, :head_width]],
        axis=0,
    )
    value_rows = jnp.concatenate(
        [own_block[:, head_width:], block_mine[:, head_width:], block_partner[:, head_width:]],
        axis=0,
    )
    scores = jnp.einsum(
        "qhd,kd->hqk", queries, key_rows, preferred_element_type=jnp.float32
    ) * head_width ** (-0.5)
    window_rows = own_block.shape[0]
    pick_rows = block_mine.shape[0]
    row_index = jnp.arange(token_rows, dtype=jnp.int32)
    column = jnp.arange(window_rows, dtype=jnp.int32)
    causal = (column[None, :] <= row_index[:, None] + token_rows) & (
        (column[None, :] >= token_rows) | (global_index > 0)
    )
    first_ok = mine[0] < my_block - 1
    second_ok = (mine[1] < my_block - 1) & (mine[1] != mine[0])
    mine_ok = jnp.where(my_choice == 0, first_ok, second_ok)
    partner_ok = jnp.where(my_choice == 0, second_ok, first_ok)
    visible = jnp.concatenate(
        [
            causal,
            jnp.broadcast_to(mine_ok, (token_rows, pick_rows)),
            jnp.broadcast_to(partner_ok, (token_rows, pick_rows)),
        ],
        axis=1,
    )
    scores = jnp.where(visible[None], scores, -jnp.inf)
    highest = jnp.max(scores, axis=2, keepdims=True)
    probs = jnp.exp(scores - highest)
    denominator = jnp.sum(probs, axis=2, keepdims=True)
    mixed = (
        jnp.einsum(
            "hqk,kd->hqd",
            probs.astype(jnp.bfloat16),
            value_rows,
            preferred_element_type=jnp.float32,
        )
        / denominator
    )
    return jnp.transpose(mixed, (1, 0, 2)).reshape(token_rows, -1).astype(jnp.bfloat16)


def solution(mesh):
    return jax.shard_map(
        per_device,
        mesh=mesh,
        in_specs=(P(("ctx", "fsdp"), None), P("fsdp", None), P("fsdp", None), P("fsdp", None), P()),
        out_specs=P(("ctx", "fsdp"), None),
        check_vma=False,
    )
```

```python
import jax
import jax.numpy as jnp
from jax import lax
from jax.sharding import PartitionSpec as P

QH = 4


def from_behind(array, axis, by):
    peers = lax.axis_size(axis)
    pairs = [(i, i + by) for i in range(peers) if 0 <= i + by < peers]
    return lax.ppermute(array, axis, pairs)


def gather_rows(array, axis):
    peers = lax.axis_size(axis)
    spread = jnp.broadcast_to(array[None], (peers,) + array.shape)
    got = lax.all_to_all(spread, axis, split_axis=0, concat_axis=0, tiled=True)
    return got.reshape((peers * array.shape[0],) + array.shape[1:])


def ring_gather_rows(array, axis):
    peers = lax.axis_size(axis)
    chips = peers // 2
    shift_pairs = lambda by: [(i, (i + by) % peers) for i in range(peers)]
    ahead = array
    behind = array
    from_ahead = []
    from_behind_ = []
    for step in range(chips // 2):
        ahead = lax.ppermute(ahead, axis, shift_pairs(2))
        from_ahead.append(ahead)
        if step < chips // 2 - 1:
            behind = lax.ppermute(behind, axis, shift_pairs(-2))
            from_behind_.append(behind)
    mine = jnp.stack(from_ahead[::-1] + [array] + from_behind_, axis=0)
    other = lax.ppermute(mine, axis, [(i, i ^ 1) for i in range(peers)])
    lane = lax.axis_index(axis)
    start = (lane // 2 - chips // 2) % chips

    def natural(stacked):
        doubled = jnp.concatenate([stacked, stacked], axis=0)
        return lax.dynamic_slice_in_dim(doubled, chips - start, chips, 0)

    mine, other = natural(mine), natural(other)
    core = lane % 2
    first = jnp.where(core == 0, mine, other)
    second = jnp.where(core == 0, other, mine)
    full = jnp.stack([first, second], axis=1)
    return full.reshape((peers * array.shape[0],) + array.shape[1:])


def swap_partner(array, axis):
    peers = lax.axis_size(axis)
    pairs = [(i, i ^ 1) for i in range(peers)]
    return lax.ppermute(array, axis, pairs)


def per_device(tokens, query_weight, key_weight, value_weight, chosen):
    token_rows = tokens.shape[0]
    head_width = key_weight.shape[1]
    lane_count = lax.axis_size("fsdp")
    lane_index = lax.axis_index("fsdp")
    group_index = lax.axis_index("ctx")
    blocks_group = lane_count // 2
    my_block = group_index * blocks_group + lane_index // 2
    global_index = group_index * lane_count + lane_index

    kv_weight = lax.all_gather(
        jnp.concatenate([key_weight, value_weight], axis=1), "fsdp", axis=0, tiled=True
    )
    kv_f32 = jnp.dot(tokens, kv_weight, preferred_element_type=jnp.float32)
    key_value = kv_f32.astype(jnp.bfloat16)

    candidates = lax.all_gather(key_value[None], "ctx", axis=0, tiled=True)
    before_pair = from_behind(key_value, ("ctx", "fsdp"), 1)
    own_block = jnp.concatenate([before_pair, key_value], axis=0)

    query_weight, key_value = lax.optimization_barrier((query_weight, key_value))
    q_weight = ring_gather_rows(query_weight, "fsdp")
    queries = jnp.dot(tokens, q_weight, preferred_element_type=jnp.float32)
    queries = queries.astype(jnp.bfloat16).reshape(token_rows, QH, head_width)

    queries, chosen = lax.optimization_barrier((queries, chosen))

    dest_block = group_index * blocks_group + jnp.arange(lane_count, dtype=jnp.int32) // 2
    dest_pick = chosen[dest_block, jnp.arange(lane_count, dtype=jnp.int32) % 2]
    outgoing = jnp.take(candidates, dest_pick // blocks_group, axis=0, mode="clip")
    incoming = lax.all_to_all(outgoing, "fsdp", split_axis=0, concat_axis=0, tiled=True)

    mine = lax.dynamic_index_in_dim(chosen, my_block, 0, keepdims=False)
    my_choice = lane_index % 2
    my_pick = jnp.where(my_choice == 0, mine[0], mine[1])
    place = my_pick % blocks_group * 2
    block_mine = lax.dynamic_slice_in_dim(incoming, place, 2, 0).reshape(
        2 * token_rows, 2 * head_width
    )
    block_partner = swap_partner(block_mine, "fsdp")

    key_rows = jnp.concatenate(
        [own_block[:, :head_width], block_mine[:, :head_width], block_partner[:, :head_width]],
        axis=0,
    )
    value_rows = jnp.concatenate(
        [own_block[:, head_width:], block_mine[:, head_width:], block_partner[:, head_width:]],
        axis=0,
    )
    scores = jnp.einsum(
        "qhd,kd->hqk", queries, key_rows, preferred_element_type=jnp.float32
    ) * head_width ** (-0.5)
    window_rows = own_block.shape[0]
    pick_rows = block_mine.shape[0]
    row_index = jnp.arange(token_rows, dtype=jnp.int32)
    column = jnp.arange(window_rows, dtype=jnp.int32)
    causal = (column[None, :] <= row_index[:, None] + token_rows) & (
        (column[None, :] >= token_rows) | (global_index > 0)
    )
    first_ok = mine[0] < my_block - 1
    second_ok = (mine[1] < my_block - 1) & (mine[1] != mine[0])
    mine_ok = jnp.where(my_choice == 0, first_ok, second_ok)
    partner_ok = jnp.where(my_choice == 0, second_ok, first_ok)
    visible = jnp.concatenate(
        [
            causal,
            jnp.broadcast_to(mine_ok, (token_rows, pick_rows)),
            jnp.broadcast_to(partner_ok, (token_rows, pick_rows)),
        ],
        axis=1,
    )
    scores = jnp.where(visible[None], scores, -jnp.inf)
    highest = jnp.max(scores, axis=2, keepdims=True)
    probs = jnp.exp(scores - highest)
    denominator = jnp.sum(probs, axis=2, keepdims=True)
    mixed = (
        jnp.einsum(
            "hqk,kd->hqd",
            probs.astype(jnp.bfloat16),
            value_rows,
            preferred_element_type=jnp.float32,
        )
        / denominator
    )
    return jnp.transpose(mixed, (1, 0, 2)).reshape(token_rows, -1).astype(jnp.bfloat16)


def solution(mesh):
    return jax.shard_map(
        per_device,
        mesh=mesh,
        in_specs=(P(("ctx", "fsdp"), None), P("fsdp", None), P("fsdp", None), P("fsdp", None), P()),
        out_specs=P(("ctx", "fsdp"), None),
        check_vma=False,
    )
```

```python
import jax
import jax.numpy as jnp
from jax import lax
from jax.sharding import Mesh, PartitionSpec as P

QH = 4


def from_behind(array, axis, by):
    peers = lax.axis_size(axis)
    pairs = [(i, i + by) for i in range(peers) if 0 <= i + by < peers]
    return lax.ppermute(array, axis, pairs)


def gather_rows(array, axis):
    peers = lax.axis_size(axis)
    spread = jnp.broadcast_to(array[None], (peers,) + array.shape)
    got = lax.all_to_all(spread, axis, split_axis=0, concat_axis=0, tiled=True)
    return got.reshape((peers * array.shape[0],) + array.shape[1:])


def ring_gather_rows(array, axis):
    peers = lax.axis_size(axis)
    chips = peers // 2
    shift_pairs = lambda by: [(i, (i + by) % peers) for i in range(peers)]
    ahead = array
    behind = array
    from_ahead = []
    from_behind_ = []
    for step in range(chips // 2):
        ahead = lax.ppermute(ahead, axis, shift_pairs(2))
        from_ahead.append(ahead)
        if step < chips // 2 - 1:
            behind = lax.ppermute(behind, axis, shift_pairs(-2))
            from_behind_.append(behind)
    mine = jnp.stack(from_ahead[::-1] + [array] + from_behind_, axis=0)
    other = lax.ppermute(mine, axis, [(i, i ^ 1) for i in range(peers)])
    lane = lax.axis_index(axis)
    start = (lane // 2 - chips // 2) % chips

    def natural(stacked):
        doubled = jnp.concatenate([stacked, stacked], axis=0)
        return lax.dynamic_slice_in_dim(doubled, chips - start, chips, 0)

    mine, other = natural(mine), natural(other)
    core = lane % 2
    first = jnp.where(core == 0, mine, other)
    second = jnp.where(core == 0, other, mine)
    full = jnp.stack([first, second], axis=1)
    return full.reshape((peers * array.shape[0],) + array.shape[1:])


def swap_partner(array, axis):
    peers = lax.axis_size(axis)
    pairs = [(i, i ^ 1) for i in range(peers)]
    return lax.ppermute(array, axis, pairs)


def per_device(tokens, query_weight, key_weight, value_weight, chosen):
    token_rows = tokens.shape[0]
    head_width = key_weight.shape[1]
    lane_count = lax.axis_size("fsdp")
    lane_index = lax.axis_index("fsdp")
    group_index = lax.axis_index(("cy", "cx"))
    blocks_group = lane_count // 2
    my_block = group_index * blocks_group + lane_index // 2
    global_index = group_index * lane_count + lane_index

    kv_weight = lax.all_gather(
        jnp.concatenate([key_weight, value_weight], axis=1), "fsdp", axis=0, tiled=True
    )
    kv_f32 = jnp.dot(tokens, kv_weight, preferred_element_type=jnp.float32)
    key_value = kv_f32.astype(jnp.bfloat16)

    along_x = lax.all_gather(key_value[None], "cx", axis=0, tiled=True)
    candidates = lax.all_gather(along_x[None], "cy", axis=0, tiled=True).reshape(
        (-1,) + key_value.shape
    )
    before_pair = from_behind(key_value, ("cy", "cx", "fsdp"), 1)
    own_block = jnp.concatenate([before_pair, key_value], axis=0)

    query_weight, key_value = lax.optimization_barrier((query_weight, key_value))
    q_weight = ring_gather_rows(query_weight, "fsdp")
    queries = jnp.dot(tokens, q_weight, preferred_element_type=jnp.float32)
    queries = queries.astype(jnp.bfloat16).reshape(token_rows, QH, head_width)

    queries, chosen = lax.optimization_barrier((queries, chosen))

    dest_block = group_index * blocks_group + jnp.arange(lane_count, dtype=jnp.int32) // 2
    dest_pick = chosen[dest_block, jnp.arange(lane_count, dtype=jnp.int32) % 2]
    outgoing = jnp.take(candidates, dest_pick // blocks_group, axis=0, mode="clip")
    incoming = lax.all_to_all(outgoing, "fsdp", split_axis=0, concat_axis=0, tiled=True)

    mine = lax.dynamic_index_in_dim(chosen, my_block, 0, keepdims=False)
    my_choice = lane_index % 2
    my_pick = jnp.where(my_choice == 0, mine[0], mine[1])
    place = my_pick % blocks_group * 2
    block_mine = lax.dynamic_slice_in_dim(incoming, place, 2, 0).reshape(
        2 * token_rows, 2 * head_width
    )
    block_partner = swap_partner(block_mine, "fsdp")

    key_rows = jnp.concatenate(
        [own_block[:, :head_width], block_mine[:, :head_width], block_partner[:, :head_width]],
        axis=0,
    )
    value_rows = jnp.concatenate(
        [own_block[:, head_width:], block_mine[:, head_width:], block_partner[:, head_width:]],
        axis=0,
    )
    scores = jnp.einsum(
        "qhd,kd->hqk", queries, key_rows, preferred_element_type=jnp.float32
    ) * head_width ** (-0.5)
    window_rows = own_block.shape[0]
    pick_rows = block_mine.shape[0]
    row_index = jnp.arange(token_rows, dtype=jnp.int32)
    column = jnp.arange(window_rows, dtype=jnp.int32)
    causal = (column[None, :] <= row_index[:, None] + token_rows) & (
        (column[None, :] >= token_rows) | (global_index > 0)
    )
    first_ok = mine[0] < my_block - 1
    second_ok = (mine[1] < my_block - 1) & (mine[1] != mine[0])
    mine_ok = jnp.where(my_choice == 0, first_ok, second_ok)
    partner_ok = jnp.where(my_choice == 0, second_ok, first_ok)
    visible = jnp.concatenate(
        [
            causal,
            jnp.broadcast_to(mine_ok, (token_rows, pick_rows)),
            jnp.broadcast_to(partner_ok, (token_rows, pick_rows)),
        ],
        axis=1,
    )
    scores = jnp.where(visible[None], scores, -jnp.inf)
    highest = jnp.max(scores, axis=2, keepdims=True)
    probs = jnp.exp(scores - highest)
    denominator = jnp.sum(probs, axis=2, keepdims=True)
    mixed = (
        jnp.einsum(
            "hqk,kd->hqd",
            probs.astype(jnp.bfloat16),
            value_rows,
            preferred_element_type=jnp.float32,
        )
        / denominator
    )
    return jnp.transpose(mixed, (1, 0, 2)).reshape(token_rows, -1).astype(jnp.bfloat16)


def split_ctx(mesh):
    column = mesh.devices[:, 0]
    coords = [getattr(device, "coords", None) for device in column]
    if any(c is None for c in coords):
        across = 1
    else:
        across = len({c[0] for c in coords})
    groups, lanes = mesh.devices.shape
    return Mesh(mesh.devices.reshape(groups // across, across, lanes), ("cy", "cx", "fsdp"))


def solution(mesh):
    split = split_ctx(mesh)
    rows = P(("cy", "cx", "fsdp"), None)
    return jax.shard_map(
        per_device,
        mesh=split,
        in_specs=(rows, P("fsdp", None), P("fsdp", None), P("fsdp", None), P()),
        out_specs=rows,
        check_vma=False,
    )
```

```python
import jax
import jax.numpy as jnp
from jax import lax
from jax.sharding import Mesh, PartitionSpec as P

QH = 4


def from_behind(array, axis, by):
    peers = lax.axis_size(axis)
    pairs = [(i, i + by) for i in range(peers) if 0 <= i + by < peers]
    return lax.ppermute(array, axis, pairs)


def gather_rows(array, axis):
    peers = lax.axis_size(axis)
    spread = jnp.broadcast_to(array[None], (peers,) + array.shape)
    got = lax.all_to_all(spread, axis, split_axis=0, concat_axis=0, tiled=True)
    return got.reshape((peers * array.shape[0],) + array.shape[1:])


def ring_gather_rows(array, axis, early_steps, tied):
    peers = lax.axis_size(axis)
    chips = peers // 2
    shift_pairs = lambda by: [(i, (i + by) % peers) for i in range(peers)]
    ahead = array
    behind = array
    from_ahead = []
    from_behind_ = []
    for step in range(chips // 2):
        if step == early_steps:
            ahead, behind, tied = lax.optimization_barrier((ahead, behind, tied))
            from_ahead[-1] = ahead
            if from_behind_:
                from_behind_[-1] = behind
        ahead = lax.ppermute(ahead, axis, shift_pairs(2))
        from_ahead.append(ahead)
        if step < chips // 2 - 1:
            behind = lax.ppermute(behind, axis, shift_pairs(-2))
            from_behind_.append(behind)
    mine = jnp.stack(from_ahead[::-1] + [array] + from_behind_, axis=0)
    other = lax.ppermute(mine, axis, [(i, i ^ 1) for i in range(peers)])
    lane = lax.axis_index(axis)
    start = (lane // 2 - chips // 2) % chips

    def natural(stacked):
        doubled = jnp.concatenate([stacked, stacked], axis=0)
        return lax.dynamic_slice_in_dim(doubled, chips - start, chips, 0)

    mine, other = natural(mine), natural(other)
    core = lane % 2
    first = jnp.where(core == 0, mine, other)
    second = jnp.where(core == 0, other, mine)
    full = jnp.stack([first, second], axis=1)
    return full.reshape((peers * array.shape[0],) + array.shape[1:]), tied


def swap_partner(array, axis):
    peers = lax.axis_size(axis)
    pairs = [(i, i ^ 1) for i in range(peers)]
    return lax.ppermute(array, axis, pairs)


def per_device(tokens, query_weight, key_weight, value_weight, chosen):
    token_rows = tokens.shape[0]
    head_width = key_weight.shape[1]
    lane_count = lax.axis_size("fsdp")
    lane_index = lax.axis_index("fsdp")
    group_index = lax.axis_index(("cy", "cx"))
    blocks_group = lane_count // 2
    my_block = group_index * blocks_group + lane_index // 2
    global_index = group_index * lane_count + lane_index

    kv_weight = lax.all_gather(
        jnp.concatenate([key_weight, value_weight], axis=1), "fsdp", axis=0, tiled=True
    )
    q_weight, kv_weight = ring_gather_rows(query_weight, "fsdp", 2, kv_weight)
    kv_f32 = jnp.dot(tokens, kv_weight, preferred_element_type=jnp.float32)
    key_value = kv_f32.astype(jnp.bfloat16)

    along_x = lax.all_gather(key_value[None], "cx", axis=0, tiled=True)
    candidates = lax.all_gather(along_x[None], "cy", axis=0, tiled=True).reshape(
        (-1,) + key_value.shape
    )
    before_pair = from_behind(key_value, ("cy", "cx", "fsdp"), 1)
    own_block = jnp.concatenate([before_pair, key_value], axis=0)

    queries = jnp.dot(tokens, q_weight, preferred_element_type=jnp.float32)
    queries = queries.astype(jnp.bfloat16).reshape(token_rows, QH, head_width)

    queries, chosen = lax.optimization_barrier((queries, chosen))

    dest_block = group_index * blocks_group + jnp.arange(lane_count, dtype=jnp.int32) // 2
    dest_pick = chosen[dest_block, jnp.arange(lane_count, dtype=jnp.int32) % 2]
    outgoing = jnp.take(candidates, dest_pick // blocks_group, axis=0, mode="clip")
    incoming = lax.all_to_all(outgoing, "fsdp", split_axis=0, concat_axis=0, tiled=True)

    mine = lax.dynamic_index_in_dim(chosen, my_block, 0, keepdims=False)
    my_choice = lane_index % 2
    my_pick = jnp.where(my_choice == 0, mine[0], mine[1])
    place = my_pick % blocks_group * 2
    block_mine = lax.dynamic_slice_in_dim(incoming, place, 2, 0).reshape(
        2 * token_rows, 2 * head_width
    )
    block_partner = swap_partner(block_mine, "fsdp")

    key_rows = jnp.concatenate(
        [own_block[:, :head_width], block_mine[:, :head_width], block_partner[:, :head_width]],
        axis=0,
    )
    value_rows = jnp.concatenate(
        [own_block[:, head_width:], block_mine[:, head_width:], block_partner[:, head_width:]],
        axis=0,
    )
    scores = jnp.einsum(
        "qhd,kd->hqk", queries, key_rows, preferred_element_type=jnp.float32
    ) * head_width ** (-0.5)
    window_rows = own_block.shape[0]
    pick_rows = block_mine.shape[0]
    row_index = jnp.arange(token_rows, dtype=jnp.int32)
    column = jnp.arange(window_rows, dtype=jnp.int32)
    causal = (column[None, :] <= row_index[:, None] + token_rows) & (
        (column[None, :] >= token_rows) | (global_index > 0)
    )
    first_ok = mine[0] < my_block - 1
    second_ok = (mine[1] < my_block - 1) & (mine[1] != mine[0])
    mine_ok = jnp.where(my_choice == 0, first_ok, second_ok)
    partner_ok = jnp.where(my_choice == 0, second_ok, first_ok)
    visible = jnp.concatenate(
        [
            causal,
            jnp.broadcast_to(mine_ok, (token_rows, pick_rows)),
            jnp.broadcast_to(partner_ok, (token_rows, pick_rows)),
        ],
        axis=1,
    )
    scores = jnp.where(visible[None], scores, -jnp.inf)
    highest = jnp.max(scores, axis=2, keepdims=True)
    probs = jnp.exp(scores - highest)
    denominator = jnp.sum(probs, axis=2, keepdims=True)
    mixed = (
        jnp.einsum(
            "hqk,kd->hqd",
            probs.astype(jnp.bfloat16),
            value_rows,
            preferred_element_type=jnp.float32,
        )
        / denominator
    )
    return jnp.transpose(mixed, (1, 0, 2)).reshape(token_rows, -1).astype(jnp.bfloat16)


def split_ctx(mesh):
    column = mesh.devices[:, 0]
    coords = [getattr(device, "coords", None) for device in column]
    if any(c is None for c in coords):
        across = 1
    else:
        across = len({c[0] for c in coords})
    groups, lanes = mesh.devices.shape
    return Mesh(mesh.devices.reshape(groups // across, across, lanes), ("cy", "cx", "fsdp"))


def solution(mesh):
    split = split_ctx(mesh)
    rows = P(("cy", "cx", "fsdp"), None)
    return jax.shard_map(
        per_device,
        mesh=split,
        in_specs=(rows, P("fsdp", None), P("fsdp", None), P("fsdp", None), P()),
        out_specs=rows,
        check_vma=False,
    )
```

```python
import jax
import jax.numpy as jnp
from jax import lax
from jax.sharding import Mesh, PartitionSpec as P

QH = 4


def from_behind(array, axis, by):
    peers = lax.axis_size(axis)
    pairs = [(i, i + by) for i in range(peers) if 0 <= i + by < peers]
    return lax.ppermute(array, axis, pairs)


def gather_rows(array, axis):
    peers = lax.axis_size(axis)
    spread = jnp.broadcast_to(array[None], (peers,) + array.shape)
    got = lax.all_to_all(spread, axis, split_axis=0, concat_axis=0, tiled=True)
    return got.reshape((peers * array.shape[0],) + array.shape[1:])


def ring_gather_rows(array, axis, early_steps, tied):
    peers = lax.axis_size(axis)
    chips = peers // 2
    shift_pairs = lambda by: [(i, (i + by) % peers) for i in range(peers)]
    ahead = array
    behind = array
    from_ahead = []
    from_behind_ = []
    for step in range(chips // 2):
        if step == early_steps:
            ahead, behind, tied = lax.optimization_barrier((ahead, behind, tied))
            from_ahead[-1] = ahead
            if from_behind_:
                from_behind_[-1] = behind
        ahead = lax.ppermute(ahead, axis, shift_pairs(2))
        from_ahead.append(ahead)
        if step < chips // 2 - 1:
            behind = lax.ppermute(behind, axis, shift_pairs(-2))
            from_behind_.append(behind)
    mine = jnp.stack(from_ahead[::-1] + [array] + from_behind_, axis=0)
    other = lax.ppermute(mine, axis, [(i, i ^ 1) for i in range(peers)])
    lane = lax.axis_index(axis)
    start = (lane // 2 - chips // 2) % chips

    def natural(stacked):
        doubled = jnp.concatenate([stacked, stacked], axis=0)
        return lax.dynamic_slice_in_dim(doubled, chips - start, chips, 0)

    mine, other = natural(mine), natural(other)
    core = lane % 2
    first = jnp.where(core == 0, mine, other)
    second = jnp.where(core == 0, other, mine)
    full = jnp.stack([first, second], axis=1)
    return full.reshape((peers * array.shape[0],) + array.shape[1:]), tied


def swap_partner(array, axis):
    peers = lax.axis_size(axis)
    pairs = [(i, i ^ 1) for i in range(peers)]
    return lax.ppermute(array, axis, pairs)


def per_device(tokens, query_weight, key_weight, value_weight, chosen):
    token_rows = tokens.shape[0]
    head_width = key_weight.shape[1]
    lane_count = lax.axis_size("fsdp")
    lane_index = lax.axis_index("fsdp")
    group_index = lax.axis_index(("cy", "cx"))
    blocks_group = lane_count // 2
    my_block = group_index * blocks_group + lane_index // 2
    global_index = group_index * lane_count + lane_index

    kv_weight = lax.all_gather(
        jnp.concatenate([key_weight, value_weight], axis=1), "fsdp", axis=0, tiled=True
    )
    q_weight, kv_weight = ring_gather_rows(query_weight, "fsdp", 2, kv_weight)
    kv_f32 = jnp.dot(tokens, kv_weight, preferred_element_type=jnp.float32)
    key_value = kv_f32.astype(jnp.bfloat16)

    along_x = lax.all_gather(key_value[None], "cx", axis=0, tiled=True)
    candidates = lax.all_gather(along_x[None], "cy", axis=0, tiled=True).reshape(
        (-1,) + key_value.shape
    )
    before_pair = from_behind(key_value, ("cy", "cx", "fsdp"), 1)
    own_block = jnp.concatenate([before_pair, key_value], axis=0)

    queries = jnp.dot(tokens, q_weight, preferred_element_type=jnp.float32)
    queries = queries.astype(jnp.bfloat16).reshape(token_rows, QH, head_width)

    queries, chosen = lax.optimization_barrier((queries, chosen))

    dest_block = group_index * blocks_group + jnp.arange(lane_count, dtype=jnp.int32) // 2
    dest_pick = chosen[dest_block, jnp.arange(lane_count, dtype=jnp.int32) % 2]
    sources = candidates.shape[0]
    pick_hot = (
        (dest_pick // blocks_group)[:, None] == jnp.arange(sources, dtype=jnp.int32)[None, :]
    ).astype(candidates.dtype)
    outgoing = jnp.dot(
        pick_hot, candidates.reshape(sources, -1), preferred_element_type=jnp.float32
    ).astype(candidates.dtype).reshape((lane_count,) + candidates.shape[1:])
    incoming = lax.all_to_all(outgoing, "fsdp", split_axis=0, concat_axis=0, tiled=True)

    mine = lax.dynamic_index_in_dim(chosen, my_block, 0, keepdims=False)
    my_choice = lane_index % 2
    my_pick = jnp.where(my_choice == 0, mine[0], mine[1])
    place = my_pick % blocks_group * 2
    block_mine = lax.dynamic_slice_in_dim(incoming, place, 2, 0).reshape(
        2 * token_rows, 2 * head_width
    )
    block_partner = swap_partner(block_mine, "fsdp")

    scale = head_width ** (-0.5)
    scores = jnp.concatenate(
        [
            jnp.einsum(
                "qhd,kd->hqk", queries, rows[:, :head_width], preferred_element_type=jnp.float32
            )
            for rows in (own_block, block_mine, block_partner)
        ],
        axis=2,
    ) * scale
    value_rows = jnp.concatenate(
        [own_block[:, head_width:], block_mine[:, head_width:], block_partner[:, head_width:]],
        axis=0,
    )
    window_rows = own_block.shape[0]
    pick_rows = block_mine.shape[0]
    row_index = jnp.arange(token_rows, dtype=jnp.int32)
    column = jnp.arange(window_rows, dtype=jnp.int32)
    causal = (column[None, :] <= row_index[:, None] + token_rows) & (
        (column[None, :] >= token_rows) | (global_index > 0)
    )
    first_ok = mine[0] < my_block - 1
    second_ok = (mine[1] < my_block - 1) & (mine[1] != mine[0])
    mine_ok = jnp.where(my_choice == 0, first_ok, second_ok)
    partner_ok = jnp.where(my_choice == 0, second_ok, first_ok)
    visible = jnp.concatenate(
        [
            causal,
            jnp.broadcast_to(mine_ok, (token_rows, pick_rows)),
            jnp.broadcast_to(partner_ok, (token_rows, pick_rows)),
        ],
        axis=1,
    )
    scores = jnp.where(visible[None], scores, -jnp.inf)
    highest = jnp.max(scores, axis=2, keepdims=True)
    probs = jnp.exp(scores - highest)
    denominator = jnp.sum(probs, axis=2, keepdims=True)
    mixed = (
        jnp.einsum(
            "hqk,kd->hqd",
            probs.astype(jnp.bfloat16),
            value_rows,
            preferred_element_type=jnp.float32,
        )
        / denominator
    )
    return jnp.transpose(mixed, (1, 0, 2)).reshape(token_rows, -1).astype(jnp.bfloat16)


def split_ctx(mesh):
    column = mesh.devices[:, 0]
    coords = [getattr(device, "coords", None) for device in column]
    if any(c is None for c in coords):
        across = 1
    else:
        across = len({c[0] for c in coords})
    groups, lanes = mesh.devices.shape
    return Mesh(mesh.devices.reshape(groups // across, across, lanes), ("cy", "cx", "fsdp"))


def solution(mesh):
    split = split_ctx(mesh)
    rows = P(("cy", "cx", "fsdp"), None)
    return jax.shard_map(
        per_device,
        mesh=split,
        in_specs=(rows, P("fsdp", None), P("fsdp", None), P("fsdp", None), P()),
        out_specs=rows,
        check_vma=False,
    )
```

```python
import jax
import jax.numpy as jnp
from jax import lax
from jax.sharding import Mesh, PartitionSpec as P

QH = 4


def from_behind(array, axis, by):
    peers = lax.axis_size(axis)
    pairs = [(i, i + by) for i in range(peers) if 0 <= i + by < peers]
    return lax.ppermute(array, axis, pairs)


def gather_rows(array, axis):
    peers = lax.axis_size(axis)
    spread = jnp.broadcast_to(array[None], (peers,) + array.shape)
    got = lax.all_to_all(spread, axis, split_axis=0, concat_axis=0, tiled=True)
    return got.reshape((peers * array.shape[0],) + array.shape[1:])


def ring_gather_rows(array, axis, early_steps, tied):
    peers = lax.axis_size(axis)
    chips = peers // 2
    shift_pairs = lambda by: [(i, (i + by) % peers) for i in range(peers)]
    ahead = array
    behind = array
    from_ahead = []
    from_behind_ = []
    for step in range(chips // 2):
        if step == early_steps:
            ahead, behind, tied = lax.optimization_barrier((ahead, behind, tied))
            from_ahead[-1] = ahead
            if from_behind_:
                from_behind_[-1] = behind
        ahead = lax.ppermute(ahead, axis, shift_pairs(2))
        from_ahead.append(ahead)
        if step < chips // 2 - 1:
            behind = lax.ppermute(behind, axis, shift_pairs(-2))
            from_behind_.append(behind)
    mine = jnp.stack(from_ahead[::-1] + [array] + from_behind_, axis=0)
    other = lax.ppermute(mine, axis, [(i, i ^ 1) for i in range(peers)])
    lane = lax.axis_index(axis)
    start = (lane // 2 - chips // 2) % chips

    def natural(stacked):
        doubled = jnp.concatenate([stacked, stacked], axis=0)
        return lax.dynamic_slice_in_dim(doubled, chips - start, chips, 0)

    mine, other = natural(mine), natural(other)
    core = lane % 2
    first = jnp.where(core == 0, mine, other)
    second = jnp.where(core == 0, other, mine)
    full = jnp.stack([first, second], axis=1)
    return full.reshape((peers * array.shape[0],) + array.shape[1:]), tied


def swap_partner(array, axis):
    peers = lax.axis_size(axis)
    pairs = [(i, i ^ 1) for i in range(peers)]
    return lax.ppermute(array, axis, pairs)


def per_device(tokens, query_weight, key_weight, value_weight, chosen):
    token_rows = tokens.shape[0]
    head_width = key_weight.shape[1]
    lane_count = lax.axis_size("fsdp")
    lane_index = lax.axis_index("fsdp")
    group_index = lax.axis_index(("cy", "cx"))
    blocks_group = lane_count // 2
    my_block = group_index * blocks_group + lane_index // 2
    global_index = group_index * lane_count + lane_index

    kv_weight = lax.all_gather(
        jnp.concatenate([key_weight, value_weight], axis=1), "fsdp", axis=0, tiled=True
    )
    q_weight, kv_weight = ring_gather_rows(query_weight, "fsdp", 2, kv_weight)
    kv_f32 = jnp.dot(tokens, kv_weight, preferred_element_type=jnp.float32)
    key_value = kv_f32.astype(jnp.bfloat16)

    before_pair = from_behind(key_value, ("cy", "cx", "fsdp"), 1)
    along_x = lax.all_gather(key_value[None], "cx", axis=0, tiled=True)
    along_x, before_pair = lax.optimization_barrier((along_x, before_pair))
    candidates = lax.all_gather(along_x[None], "cy", axis=0, tiled=True).reshape(
        (-1,) + key_value.shape
    )
    own_block = jnp.concatenate([before_pair, key_value], axis=0)

    queries = jnp.dot(tokens, q_weight, preferred_element_type=jnp.float32)
    queries = queries.astype(jnp.bfloat16).reshape(token_rows, QH, head_width)

    queries, chosen = lax.optimization_barrier((queries, chosen))

    dest_block = group_index * blocks_group + jnp.arange(lane_count, dtype=jnp.int32) // 2
    dest_pick = chosen[dest_block, jnp.arange(lane_count, dtype=jnp.int32) % 2]
    sources = candidates.shape[0]
    pick_hot = (
        (dest_pick // blocks_group)[:, None] == jnp.arange(sources, dtype=jnp.int32)[None, :]
    ).astype(candidates.dtype)
    outgoing = jnp.dot(
        pick_hot, candidates.reshape(sources, -1), preferred_element_type=jnp.float32
    ).astype(candidates.dtype).reshape((lane_count,) + candidates.shape[1:])
    incoming = lax.all_to_all(outgoing, "fsdp", split_axis=0, concat_axis=0, tiled=True)

    mine = lax.dynamic_index_in_dim(chosen, my_block, 0, keepdims=False)
    my_choice = lane_index % 2
    my_pick = jnp.where(my_choice == 0, mine[0], mine[1])
    place = my_pick % blocks_group * 2
    block_mine = lax.dynamic_slice_in_dim(incoming, place, 2, 0).reshape(
        2 * token_rows, 2 * head_width
    )
    block_partner = swap_partner(block_mine, "fsdp")

    scale = head_width ** (-0.5)
    scores = jnp.concatenate(
        [
            jnp.einsum(
                "qhd,kd->hqk", queries, rows[:, :head_width], preferred_element_type=jnp.float32
            )
            for rows in (own_block, block_mine, block_partner)
        ],
        axis=2,
    ) * scale
    value_rows = jnp.concatenate(
        [own_block[:, head_width:], block_mine[:, head_width:], block_partner[:, head_width:]],
        axis=0,
    )
    window_rows = own_block.shape[0]
    pick_rows = block_mine.shape[0]
    row_index = jnp.arange(token_rows, dtype=jnp.int32)
    column = jnp.arange(window_rows, dtype=jnp.int32)
    causal = (column[None, :] <= row_index[:, None] + token_rows) & (
        (column[None, :] >= token_rows) | (global_index > 0)
    )
    first_ok = mine[0] < my_block - 1
    second_ok = (mine[1] < my_block - 1) & (mine[1] != mine[0])
    mine_ok = jnp.where(my_choice == 0, first_ok, second_ok)
    partner_ok = jnp.where(my_choice == 0, second_ok, first_ok)
    visible = jnp.concatenate(
        [
            causal,
            jnp.broadcast_to(mine_ok, (token_rows, pick_rows)),
            jnp.broadcast_to(partner_ok, (token_rows, pick_rows)),
        ],
        axis=1,
    )
    scores = jnp.where(visible[None], scores, -jnp.inf)
    highest = jnp.max(scores, axis=2, keepdims=True)
    probs = jnp.exp(scores - highest)
    denominator = jnp.sum(probs, axis=2, keepdims=True)
    mixed = (
        jnp.einsum(
            "hqk,kd->hqd",
            probs.astype(jnp.bfloat16),
            value_rows,
            preferred_element_type=jnp.float32,
        )
        / denominator
    )
    return jnp.transpose(mixed, (1, 0, 2)).reshape(token_rows, -1).astype(jnp.bfloat16)


def split_ctx(mesh):
    column = mesh.devices[:, 0]
    coords = [getattr(device, "coords", None) for device in column]
    if any(c is None for c in coords):
        across = 1
    else:
        across = len({c[0] for c in coords})
    groups, lanes = mesh.devices.shape
    return Mesh(mesh.devices.reshape(groups // across, across, lanes), ("cy", "cx", "fsdp"))


def solution(mesh):
    split = split_ctx(mesh)
    rows = P(("cy", "cx", "fsdp"), None)
    return jax.shard_map(
        per_device,
        mesh=split,
        in_specs=(rows, P("fsdp", None), P("fsdp", None), P("fsdp", None), P()),
        out_specs=rows,
        check_vma=False,
    )
```

```python
import jax
import jax.numpy as jnp
from jax import lax
from jax.sharding import Mesh, PartitionSpec as P

QH = 4


def from_behind(array, axis, by):
    peers = lax.axis_size(axis)
    pairs = [(i, i + by) for i in range(peers) if 0 <= i + by < peers]
    return lax.ppermute(array, axis, pairs)


def gather_rows(array, axis):
    peers = lax.axis_size(axis)
    spread = jnp.broadcast_to(array[None], (peers,) + array.shape)
    got = lax.all_to_all(spread, axis, split_axis=0, concat_axis=0, tiled=True)
    return got.reshape((peers * array.shape[0],) + array.shape[1:])


def ring_gather_rows(array, axis, early_steps, tied):
    peers = lax.axis_size(axis)
    chips = peers // 2
    shift_pairs = lambda by: [(i, (i + by) % peers) for i in range(peers)]
    ahead = array
    behind = array
    from_ahead = []
    from_behind_ = []
    for step in range(chips // 2):
        if step == early_steps:
            ahead, behind, tied = lax.optimization_barrier((ahead, behind, tied))
            from_ahead[-1] = ahead
            if from_behind_:
                from_behind_[-1] = behind
        ahead = lax.ppermute(ahead, axis, shift_pairs(2))
        from_ahead.append(ahead)
        if step < chips // 2 - 1:
            behind = lax.ppermute(behind, axis, shift_pairs(-2))
            from_behind_.append(behind)
    mine = jnp.stack(from_ahead[::-1] + [array] + from_behind_, axis=0)
    other = lax.ppermute(mine, axis, [(i, i ^ 1) for i in range(peers)])
    lane = lax.axis_index(axis)
    start = (lane // 2 - chips // 2) % chips

    def natural(stacked):
        doubled = jnp.concatenate([stacked, stacked], axis=0)
        return lax.dynamic_slice_in_dim(doubled, chips - start, chips, 0)

    mine, other = natural(mine), natural(other)
    core = lane % 2
    first = jnp.where(core == 0, mine, other)
    second = jnp.where(core == 0, other, mine)
    full = jnp.stack([first, second], axis=1)
    return full.reshape((peers * array.shape[0],) + array.shape[1:]), tied


def swap_partner(array, axis):
    peers = lax.axis_size(axis)
    pairs = [(i, i ^ 1) for i in range(peers)]
    return lax.ppermute(array, axis, pairs)


def per_device(tokens, query_weight, key_weight, value_weight, chosen):
    token_rows = tokens.shape[0]
    head_width = key_weight.shape[1]
    lane_count = lax.axis_size("fsdp")
    lane_index = lax.axis_index("fsdp")
    group_index = lax.axis_index(("cy", "cx"))
    blocks_group = lane_count // 2
    my_block = group_index * blocks_group + lane_index // 2
    global_index = group_index * lane_count + lane_index

    kv_weight = lax.all_gather(
        jnp.concatenate([key_weight, value_weight], axis=1), "fsdp", axis=0, tiled=True
    )
    q_weight, kv_weight = ring_gather_rows(query_weight, "fsdp", 2, kv_weight)
    kv_f32 = jnp.dot(tokens, kv_weight, preferred_element_type=jnp.float32)
    key_value = kv_f32.astype(jnp.bfloat16)

    along_x = lax.all_gather(key_value[None], "cx", axis=0, tiled=True)
    candidates = lax.all_gather(along_x[None], "cy", axis=0, tiled=True).reshape(
        (-1,) + key_value.shape
    )
    before_pair = from_behind(key_value, ("cy", "cx", "fsdp"), 1)
    own_block = jnp.concatenate([before_pair, key_value], axis=0)

    queries = jnp.dot(tokens, q_weight, preferred_element_type=jnp.float32)
    queries = queries.astype(jnp.bfloat16).reshape(token_rows, QH, head_width)

    queries, chosen = lax.optimization_barrier((queries, chosen))

    dest_block = group_index * blocks_group + jnp.arange(lane_count, dtype=jnp.int32) // 2
    dest_pick = chosen[dest_block, jnp.arange(lane_count, dtype=jnp.int32) % 2]
    outgoing = jnp.take(candidates, dest_pick // blocks_group, axis=0, mode="clip")
    incoming = lax.all_to_all(outgoing, "fsdp", split_axis=0, concat_axis=0, tiled=True)

    mine = lax.dynamic_index_in_dim(chosen, my_block, 0, keepdims=False)
    my_choice = lane_index % 2
    my_pick = jnp.where(my_choice == 0, mine[0], mine[1])
    place = my_pick % blocks_group * 2
    block_mine = lax.dynamic_slice_in_dim(incoming, place, 2, 0).reshape(
        2 * token_rows, 2 * head_width
    )
    block_partner = swap_partner(block_mine, "fsdp")

    scale = head_width ** (-0.5)
    scores = jnp.concatenate(
        [
            jnp.einsum(
                "qhd,kd->hqk", queries, rows[:, :head_width], preferred_element_type=jnp.float32
            )
            for rows in (own_block, block_mine, block_partner)
        ],
        axis=2,
    ) * scale
    value_rows = jnp.concatenate(
        [own_block[:, head_width:], block_mine[:, head_width:], block_partner[:, head_width:]],
        axis=0,
    )
    window_rows = own_block.shape[0]
    pick_rows = block_mine.shape[0]
    row_index = jnp.arange(token_rows, dtype=jnp.int32)
    column = jnp.arange(window_rows, dtype=jnp.int32)
    causal = (column[None, :] <= row_index[:, None] + token_rows) & (
        (column[None, :] >= token_rows) | (global_index > 0)
    )
    first_ok = mine[0] < my_block - 1
    second_ok = (mine[1] < my_block - 1) & (mine[1] != mine[0])
    mine_ok = jnp.where(my_choice == 0, first_ok, second_ok)
    partner_ok = jnp.where(my_choice == 0, second_ok, first_ok)
    visible = jnp.concatenate(
        [
            causal,
            jnp.broadcast_to(mine_ok, (token_rows, pick_rows)),
            jnp.broadcast_to(partner_ok, (token_rows, pick_rows)),
        ],
        axis=1,
    )
    scores = jnp.where(visible[None], scores, -jnp.inf)
    highest = jnp.max(scores, axis=2, keepdims=True)
    probs = jnp.exp(scores - highest)
    denominator = jnp.sum(probs, axis=2, keepdims=True)
    mixed = (
        jnp.einsum(
            "hqk,kd->hqd",
            probs.astype(jnp.bfloat16),
            value_rows,
            preferred_element_type=jnp.float32,
        )
        / denominator
    )
    return jnp.transpose(mixed, (1, 0, 2)).reshape(token_rows, -1).astype(jnp.bfloat16)


def split_ctx(mesh):
    column = mesh.devices[:, 0]
    coords = [getattr(device, "coords", None) for device in column]
    if any(c is None for c in coords):
        across = 1
    else:
        across = len({c[0] for c in coords})
    groups, lanes = mesh.devices.shape
    return Mesh(mesh.devices.reshape(groups // across, across, lanes), ("cy", "cx", "fsdp"))


def solution(mesh):
    split = split_ctx(mesh)
    rows = P(("cy", "cx", "fsdp"), None)
    return jax.shard_map(
        per_device,
        mesh=split,
        in_specs=(rows, P("fsdp", None), P("fsdp", None), P("fsdp", None), P()),
        out_specs=rows,
        check_vma=False,
    )
```

```python
import jax
import jax.numpy as jnp
from jax import lax
from jax.sharding import Mesh, PartitionSpec as P

QH = 4


def from_behind(array, axis, by):
    peers = lax.axis_size(axis)
    pairs = [(i, i + by) for i in range(peers) if 0 <= i + by < peers]
    return lax.ppermute(array, axis, pairs)


def gather_rows(array, axis):
    peers = lax.axis_size(axis)
    spread = jnp.broadcast_to(array[None], (peers,) + array.shape)
    got = lax.all_to_all(spread, axis, split_axis=0, concat_axis=0, tiled=True)
    return got.reshape((peers * array.shape[0],) + array.shape[1:])


def ring_gather_rows(array, axis, early_steps, tied):
    peers = lax.axis_size(axis)
    chips = peers // 2
    shift_pairs = lambda by: [(i, (i + by) % peers) for i in range(peers)]
    ahead = array
    behind = array
    from_ahead = []
    from_behind_ = []
    for step in range(chips // 2):
        if step == early_steps:
            ahead, behind, tied = lax.optimization_barrier((ahead, behind, tied))
            from_ahead[-1] = ahead
            if from_behind_:
                from_behind_[-1] = behind
        ahead = lax.ppermute(ahead, axis, shift_pairs(2))
        from_ahead.append(ahead)
        if step < chips // 2 - 1:
            behind = lax.ppermute(behind, axis, shift_pairs(-2))
            from_behind_.append(behind)
    mine = jnp.stack(from_ahead[::-1] + [array] + from_behind_, axis=0)
    other = lax.ppermute(mine, axis, [(i, i ^ 1) for i in range(peers)])
    lane = lax.axis_index(axis)
    start = (lane // 2 - chips // 2) % chips

    def natural(stacked):
        doubled = jnp.concatenate([stacked, stacked], axis=0)
        return lax.dynamic_slice_in_dim(doubled, chips - start, chips, 0)

    mine, other = natural(mine), natural(other)
    core = lane % 2
    first = jnp.where(core == 0, mine, other)
    second = jnp.where(core == 0, other, mine)
    full = jnp.stack([first, second], axis=1)
    return full.reshape((peers * array.shape[0],) + array.shape[1:]), tied


def shift_gather(array, axis):
    peers = lax.axis_size(axis)
    parts = [array] + [
        lax.ppermute(array, axis, [(i, (i - by) % peers) for i in range(peers)])
        for by in range(1, peers)
    ]
    stacked = jnp.stack(parts, axis=0)
    doubled = jnp.concatenate([stacked, stacked], axis=0)
    me = lax.axis_index(axis)
    return lax.dynamic_slice_in_dim(doubled, peers - me, peers, 0)


def swap_partner(array, axis):
    peers = lax.axis_size(axis)
    pairs = [(i, i ^ 1) for i in range(peers)]
    return lax.ppermute(array, axis, pairs)


def per_device(tokens, query_weight, key_weight, value_weight, chosen):
    token_rows = tokens.shape[0]
    head_width = key_weight.shape[1]
    lane_count = lax.axis_size("fsdp")
    lane_index = lax.axis_index("fsdp")
    group_index = lax.axis_index(("cy", "cx"))
    blocks_group = lane_count // 2
    my_block = group_index * blocks_group + lane_index // 2
    global_index = group_index * lane_count + lane_index

    kv_weight = lax.all_gather(
        jnp.concatenate([key_weight, value_weight], axis=1), "fsdp", axis=0, tiled=True
    )
    q_weight, kv_weight = ring_gather_rows(query_weight, "fsdp", 2, kv_weight)
    kv_f32 = jnp.dot(tokens, kv_weight, preferred_element_type=jnp.float32)
    key_value = kv_f32.astype(jnp.bfloat16)

    along_x = shift_gather(key_value, "cx")
    candidates = lax.all_gather(along_x[None], "cy", axis=0, tiled=True).reshape(
        (-1,) + key_value.shape
    )
    before_pair = from_behind(key_value, ("cy", "cx", "fsdp"), 1)
    own_block = jnp.concatenate([before_pair, key_value], axis=0)

    queries = jnp.dot(tokens, q_weight, preferred_element_type=jnp.float32)
    queries = queries.astype(jnp.bfloat16).reshape(token_rows, QH, head_width)

    queries, chosen = lax.optimization_barrier((queries, chosen))

    dest_block = group_index * blocks_group + jnp.arange(lane_count, dtype=jnp.int32) // 2
    dest_pick = chosen[dest_block, jnp.arange(lane_count, dtype=jnp.int32) % 2]
    outgoing = jnp.take(candidates, dest_pick // blocks_group, axis=0, mode="clip")
    incoming = lax.all_to_all(outgoing, "fsdp", split_axis=0, concat_axis=0, tiled=True)

    mine = lax.dynamic_index_in_dim(chosen, my_block, 0, keepdims=False)
    my_choice = lane_index % 2
    my_pick = jnp.where(my_choice == 0, mine[0], mine[1])
    place = my_pick % blocks_group * 2
    block_mine = lax.dynamic_slice_in_dim(incoming, place, 2, 0).reshape(
        2 * token_rows, 2 * head_width
    )
    block_partner = swap_partner(block_mine, "fsdp")

    scale = head_width ** (-0.5)
    scores = jnp.concatenate(
        [
            jnp.einsum(
                "qhd,kd->hqk", queries, rows[:, :head_width], preferred_element_type=jnp.float32
            )
            for rows in (own_block, block_mine, block_partner)
        ],
        axis=2,
    ) * scale
    value_rows = jnp.concatenate(
        [own_block[:, head_width:], block_mine[:, head_width:], block_partner[:, head_width:]],
        axis=0,
    )
    window_rows = own_block.shape[0]
    pick_rows = block_mine.shape[0]
    row_index = jnp.arange(token_rows, dtype=jnp.int32)
    column = jnp.arange(window_rows, dtype=jnp.int32)
    causal = (column[None, :] <= row_index[:, None] + token_rows) & (
        (column[None, :] >= token_rows) | (global_index > 0)
    )
    first_ok = mine[0] < my_block - 1
    second_ok = (mine[1] < my_block - 1) & (mine[1] != mine[0])
    mine_ok = jnp.where(my_choice == 0, first_ok, second_ok)
    partner_ok = jnp.where(my_choice == 0, second_ok, first_ok)
    visible = jnp.concatenate(
        [
            causal,
            jnp.broadcast_to(mine_ok, (token_rows, pick_rows)),
            jnp.broadcast_to(partner_ok, (token_rows, pick_rows)),
        ],
        axis=1,
    )
    scores = jnp.where(visible[None], scores, -jnp.inf)
    highest = jnp.max(scores, axis=2, keepdims=True)
    probs = jnp.exp(scores - highest)
    denominator = jnp.sum(probs, axis=2, keepdims=True)
    mixed = (
        jnp.einsum(
            "hqk,kd->hqd",
            probs.astype(jnp.bfloat16),
            value_rows,
            preferred_element_type=jnp.float32,
        )
        / denominator
    )
    return jnp.transpose(mixed, (1, 0, 2)).reshape(token_rows, -1).astype(jnp.bfloat16)


def split_ctx(mesh):
    column = mesh.devices[:, 0]
    coords = [getattr(device, "coords", None) for device in column]
    if any(c is None for c in coords):
        across = 1
    else:
        across = len({c[0] for c in coords})
    groups, lanes = mesh.devices.shape
    return Mesh(mesh.devices.reshape(groups // across, across, lanes), ("cy", "cx", "fsdp"))


def solution(mesh):
    split = split_ctx(mesh)
    rows = P(("cy", "cx", "fsdp"), None)
    return jax.shard_map(
        per_device,
        mesh=split,
        in_specs=(rows, P("fsdp", None), P("fsdp", None), P("fsdp", None), P()),
        out_specs=rows,
        check_vma=False,
    )
```

```python
import jax
import jax.numpy as jnp
from jax import lax
from jax.sharding import Mesh, PartitionSpec as P

QH = 4


def from_behind(array, axis, by):
    peers = lax.axis_size(axis)
    pairs = [(i, i + by) for i in range(peers) if 0 <= i + by < peers]
    return lax.ppermute(array, axis, pairs)


def gather_rows(array, axis):
    peers = lax.axis_size(axis)
    spread = jnp.broadcast_to(array[None], (peers,) + array.shape)
    got = lax.all_to_all(spread, axis, split_axis=0, concat_axis=0, tiled=True)
    return got.reshape((peers * array.shape[0],) + array.shape[1:])


def ring_gather_rows(array, axis, early_steps, tied):
    peers = lax.axis_size(axis)
    chips = peers // 2
    shift_pairs = lambda by: [(i, (i + by) % peers) for i in range(peers)]
    ahead = array
    behind = array
    from_ahead = []
    from_behind_ = []
    for step in range(chips // 2):
        if step == early_steps:
            ahead, behind, tied = lax.optimization_barrier((ahead, behind, tied))
            from_ahead[-1] = ahead
            if from_behind_:
                from_behind_[-1] = behind
        ahead = lax.ppermute(ahead, axis, shift_pairs(2))
        from_ahead.append(ahead)
        if step < chips // 2 - 1:
            behind = lax.ppermute(behind, axis, shift_pairs(-2))
            from_behind_.append(behind)
    mine = jnp.stack(from_ahead[::-1] + [array] + from_behind_, axis=0)
    other = lax.ppermute(mine, axis, [(i, i ^ 1) for i in range(peers)])
    lane = lax.axis_index(axis)
    start = (lane // 2 - chips // 2) % chips

    def natural(stacked):
        doubled = jnp.concatenate([stacked, stacked], axis=0)
        return lax.dynamic_slice_in_dim(doubled, chips - start, chips, 0)

    mine, other = natural(mine), natural(other)
    core = lane % 2
    first = jnp.where(core == 0, mine, other)
    second = jnp.where(core == 0, other, mine)
    full = jnp.stack([first, second], axis=1)
    return full.reshape((peers * array.shape[0],) + array.shape[1:]), tied


def swap_partner(array, axis):
    peers = lax.axis_size(axis)
    pairs = [(i, i ^ 1) for i in range(peers)]
    return lax.ppermute(array, axis, pairs)


def per_device(tokens, query_weight, key_weight, value_weight, chosen):
    token_rows = tokens.shape[0]
    head_width = key_weight.shape[1]
    lane_count = lax.axis_size("fsdp")
    lane_index = lax.axis_index("fsdp")
    group_index = lax.axis_index(("cy", "cx"))
    blocks_group = lane_count // 2
    my_block = group_index * blocks_group + lane_index // 2
    global_index = group_index * lane_count + lane_index

    kv_weight = lax.all_gather(
        jnp.stack([key_weight, value_weight], axis=0), "fsdp", axis=1, tiled=True
    )
    q_weight, kv_weight = ring_gather_rows(query_weight, "fsdp", 2, kv_weight)
    kv_f32 = jnp.einsum("td,kdc->tkc", tokens, kv_weight, preferred_element_type=jnp.float32)
    key_value = kv_f32.astype(jnp.bfloat16).reshape(token_rows, 2 * head_width)

    along_x = lax.all_gather(key_value[None], "cx", axis=0, tiled=True)
    candidates = lax.all_gather(along_x[None], "cy", axis=0, tiled=True).reshape(
        (-1,) + key_value.shape
    )
    before_pair = from_behind(key_value, ("cy", "cx", "fsdp"), 1)
    own_block = jnp.concatenate([before_pair, key_value], axis=0)

    queries = jnp.dot(tokens, q_weight, preferred_element_type=jnp.float32)
    queries = queries.astype(jnp.bfloat16).reshape(token_rows, QH, head_width)

    queries, chosen = lax.optimization_barrier((queries, chosen))

    dest_block = group_index * blocks_group + jnp.arange(lane_count, dtype=jnp.int32) // 2
    dest_pick = chosen[dest_block, jnp.arange(lane_count, dtype=jnp.int32) % 2]
    outgoing = jnp.take(candidates, dest_pick // blocks_group, axis=0, mode="clip")
    incoming = lax.all_to_all(outgoing, "fsdp", split_axis=0, concat_axis=0, tiled=True)

    mine = lax.dynamic_index_in_dim(chosen, my_block, 0, keepdims=False)
    my_choice = lane_index % 2
    my_pick = jnp.where(my_choice == 0, mine[0], mine[1])
    place = my_pick % blocks_group * 2
    block_mine = lax.dynamic_slice_in_dim(incoming, place, 2, 0).reshape(
        2 * token_rows, 2 * head_width
    )
    block_partner = swap_partner(block_mine, "fsdp")

    scale = head_width ** (-0.5)
    scores = jnp.concatenate(
        [
            jnp.einsum(
                "qhd,kd->hqk", queries, rows[:, :head_width], preferred_element_type=jnp.float32
            )
            for rows in (own_block, block_mine, block_partner)
        ],
        axis=2,
    ) * scale
    value_rows = jnp.concatenate(
        [own_block[:, head_width:], block_mine[:, head_width:], block_partner[:, head_width:]],
        axis=0,
    )
    window_rows = own_block.shape[0]
    pick_rows = block_mine.shape[0]
    row_index = jnp.arange(token_rows, dtype=jnp.int32)
    column = jnp.arange(window_rows, dtype=jnp.int32)
    causal = (column[None, :] <= row_index[:, None] + token_rows) & (
        (column[None, :] >= token_rows) | (global_index > 0)
    )
    first_ok = mine[0] < my_block - 1
    second_ok = (mine[1] < my_block - 1) & (mine[1] != mine[0])
    mine_ok = jnp.where(my_choice == 0, first_ok, second_ok)
    partner_ok = jnp.where(my_choice == 0, second_ok, first_ok)
    visible = jnp.concatenate(
        [
            causal,
            jnp.broadcast_to(mine_ok, (token_rows, pick_rows)),
            jnp.broadcast_to(partner_ok, (token_rows, pick_rows)),
        ],
        axis=1,
    )
    scores = jnp.where(visible[None], scores, -jnp.inf)
    highest = jnp.max(scores, axis=2, keepdims=True)
    probs = jnp.exp(scores - highest)
    denominator = jnp.sum(probs, axis=2, keepdims=True)
    mixed = jnp.einsum(
        "hqk,kd->qhd",
        probs.astype(jnp.bfloat16),
        value_rows,
        preferred_element_type=jnp.float32,
    ) / jnp.transpose(denominator, (1, 0, 2))
    return mixed.reshape(token_rows, -1).astype(jnp.bfloat16)


def split_ctx(mesh):
    column = mesh.devices[:, 0]
    coords = [getattr(device, "coords", None) for device in column]
    if any(c is None for c in coords):
        across = 1
    else:
        across = len({c[0] for c in coords})
    groups, lanes = mesh.devices.shape
    return Mesh(mesh.devices.reshape(groups // across, across, lanes), ("cy", "cx", "fsdp"))


def solution(mesh):
    split = split_ctx(mesh)
    rows = P(("cy", "cx", "fsdp"), None)
    return jax.shard_map(
        per_device,
        mesh=split,
        in_specs=(rows, P("fsdp", None), P("fsdp", None), P("fsdp", None), P()),
        out_specs=rows,
        check_vma=False,
    )
```

```python
import jax
import jax.numpy as jnp
from jax import lax
from jax.sharding import Mesh, PartitionSpec as P

QH = 4


def from_behind(array, axis, by):
    peers = lax.axis_size(axis)
    pairs = [(i, i + by) for i in range(peers) if 0 <= i + by < peers]
    return lax.ppermute(array, axis, pairs)


def gather_rows(array, axis):
    peers = lax.axis_size(axis)
    spread = jnp.broadcast_to(array[None], (peers,) + array.shape)
    got = lax.all_to_all(spread, axis, split_axis=0, concat_axis=0, tiled=True)
    return got.reshape((peers * array.shape[0],) + array.shape[1:])


def ring_gather_rows(array, axis, early_steps, tied):
    peers = lax.axis_size(axis)
    chips = peers // 2
    shift_pairs = lambda by: [(i, (i + by) % peers) for i in range(peers)]
    ahead = array
    behind = array
    from_ahead = []
    from_behind_ = []
    for step in range(chips // 2):
        if step == early_steps:
            ahead, behind, tied = lax.optimization_barrier((ahead, behind, tied))
            from_ahead[-1] = ahead
            if from_behind_:
                from_behind_[-1] = behind
        ahead = lax.ppermute(ahead, axis, shift_pairs(2))
        from_ahead.append(ahead)
        if step < chips // 2 - 1:
            behind = lax.ppermute(behind, axis, shift_pairs(-2))
            from_behind_.append(behind)
    mine = jnp.stack(from_ahead[::-1] + [array] + from_behind_, axis=0)
    other = lax.ppermute(mine, axis, [(i, i ^ 1) for i in range(peers)])
    lane = lax.axis_index(axis)
    start = (lane // 2 - chips // 2) % chips

    def natural(stacked):
        doubled = jnp.concatenate([stacked, stacked], axis=0)
        return lax.dynamic_slice_in_dim(doubled, chips - start, chips, 0)

    mine, other = natural(mine), natural(other)
    core = lane % 2
    first = jnp.where(core == 0, mine, other)
    second = jnp.where(core == 0, other, mine)
    full = jnp.stack([first, second], axis=1)
    return full.reshape((peers * array.shape[0],) + array.shape[1:]), tied


def swap_partner(array, axis):
    peers = lax.axis_size(axis)
    pairs = [(i, i ^ 1) for i in range(peers)]
    return lax.ppermute(array, axis, pairs)


def per_device(tokens, query_weight, key_weight, value_weight, chosen):
    token_rows = tokens.shape[0]
    head_width = key_weight.shape[1]
    lane_count = lax.axis_size("fsdp")
    lane_index = lax.axis_index("fsdp")
    group_index = lax.axis_index(("cy", "cx"))
    blocks_group = lane_count // 2
    my_block = group_index * blocks_group + lane_index // 2
    global_index = group_index * lane_count + lane_index

    kv_weight = lax.all_gather(
        jnp.concatenate([key_weight, value_weight], axis=1), "fsdp", axis=0, tiled=True
    )
    q_weight, kv_weight = ring_gather_rows(query_weight, "fsdp", 2, kv_weight)
    kv_f32 = jnp.dot(tokens, kv_weight, preferred_element_type=jnp.float32)
    key_value = kv_f32.astype(jnp.bfloat16)

    along_x = lax.all_gather(key_value[None], "cx", axis=0, tiled=True)
    candidates = lax.all_gather(along_x[None], "cy", axis=0, tiled=True).reshape(
        (-1,) + key_value.shape
    )
    before_pair = from_behind(key_value, ("cy", "cx", "fsdp"), 1)
    own_block = jnp.concatenate([before_pair, key_value], axis=0)

    queries = jnp.dot(tokens, q_weight, preferred_element_type=jnp.float32)
    queries = queries.astype(jnp.bfloat16).reshape(token_rows, QH, head_width)

    queries, chosen = lax.optimization_barrier((queries, chosen))

    dest_block = group_index * blocks_group + jnp.arange(lane_count, dtype=jnp.int32) // 2
    dest_pick = chosen[dest_block]
    outgoing = jnp.take(candidates, dest_pick // blocks_group, axis=0, mode="clip")
    incoming = lax.all_to_all(outgoing, "fsdp", split_axis=0, concat_axis=0, tiled=True)

    mine = lax.dynamic_index_in_dim(chosen, my_block, 0, keepdims=False)

    def assemble(which):
        place = mine[which] % blocks_group * 2
        return lax.dynamic_slice_in_dim(incoming[:, which], place, 2, 0).reshape(
            2 * token_rows, 2 * head_width
        )

    block_mine = assemble(0)
    block_partner = assemble(1)
    my_choice = 0

    scale = head_width ** (-0.5)
    scores = jnp.concatenate(
        [
            jnp.einsum(
                "qhd,kd->hqk", queries, rows[:, :head_width], preferred_element_type=jnp.float32
            )
            for rows in (own_block, block_mine, block_partner)
        ],
        axis=2,
    ) * scale
    value_rows = jnp.concatenate(
        [own_block[:, head_width:], block_mine[:, head_width:], block_partner[:, head_width:]],
        axis=0,
    )
    window_rows = own_block.shape[0]
    pick_rows = block_mine.shape[0]
    row_index = jnp.arange(token_rows, dtype=jnp.int32)
    column = jnp.arange(window_rows, dtype=jnp.int32)
    causal = (column[None, :] <= row_index[:, None] + token_rows) & (
        (column[None, :] >= token_rows) | (global_index > 0)
    )
    first_ok = mine[0] < my_block - 1
    second_ok = (mine[1] < my_block - 1) & (mine[1] != mine[0])
    mine_ok = jnp.where(my_choice == 0, first_ok, second_ok)
    partner_ok = jnp.where(my_choice == 0, second_ok, first_ok)
    visible = jnp.concatenate(
        [
            causal,
            jnp.broadcast_to(mine_ok, (token_rows, pick_rows)),
            jnp.broadcast_to(partner_ok, (token_rows, pick_rows)),
        ],
        axis=1,
    )
    scores = jnp.where(visible[None], scores, -jnp.inf)
    highest = jnp.max(scores, axis=2, keepdims=True)
    probs = jnp.exp(scores - highest)
    denominator = jnp.sum(probs, axis=2, keepdims=True)
    mixed = (
        jnp.einsum(
            "hqk,kd->hqd",
            probs.astype(jnp.bfloat16),
            value_rows,
            preferred_element_type=jnp.float32,
        )
        / denominator
    )
    return jnp.transpose(mixed, (1, 0, 2)).reshape(token_rows, -1).astype(jnp.bfloat16)


def split_ctx(mesh):
    column = mesh.devices[:, 0]
    coords = [getattr(device, "coords", None) for device in column]
    if any(c is None for c in coords):
        across = 1
    else:
        across = len({c[0] for c in coords})
    groups, lanes = mesh.devices.shape
    return Mesh(mesh.devices.reshape(groups // across, across, lanes), ("cy", "cx", "fsdp"))


def solution(mesh):
    split = split_ctx(mesh)
    rows = P(("cy", "cx", "fsdp"), None)
    return jax.shard_map(
        per_device,
        mesh=split,
        in_specs=(rows, P("fsdp", None), P("fsdp", None), P("fsdp", None), P()),
        out_specs=rows,
        check_vma=False,
    )
```

```python
import jax
import jax.numpy as jnp
from jax import lax
from jax.sharding import Mesh, PartitionSpec as P

QH = 4


def from_behind(array, axis, by):
    peers = lax.axis_size(axis)
    pairs = [(i, i + by) for i in range(peers) if 0 <= i + by < peers]
    return lax.ppermute(array, axis, pairs)


def gather_rows(array, axis):
    peers = lax.axis_size(axis)
    spread = jnp.broadcast_to(array[None], (peers,) + array.shape)
    got = lax.all_to_all(spread, axis, split_axis=0, concat_axis=0, tiled=True)
    return got.reshape((peers * array.shape[0],) + array.shape[1:])


def ring_gather_rows(array, axis, early_steps, tied):
    peers = lax.axis_size(axis)
    chips = peers // 2
    shift_pairs = lambda by: [(i, (i + by) % peers) for i in range(peers)]
    ahead = array
    behind = array
    from_ahead = []
    from_behind_ = []
    for step in range(chips // 2):
        if step == early_steps:
            ahead, behind, tied = lax.optimization_barrier((ahead, behind, tied))
            from_ahead[-1] = ahead
            if from_behind_:
                from_behind_[-1] = behind
        ahead = lax.ppermute(ahead, axis, shift_pairs(2))
        from_ahead.append(ahead)
        if step < chips // 2 - 1:
            behind = lax.ppermute(behind, axis, shift_pairs(-2))
            from_behind_.append(behind)
    mine = jnp.stack(from_ahead[::-1] + [array] + from_behind_, axis=0)
    other = lax.ppermute(mine, axis, [(i, i ^ 1) for i in range(peers)])
    lane = lax.axis_index(axis)
    start = (lane // 2 - chips // 2) % chips

    def natural(stacked):
        doubled = jnp.concatenate([stacked, stacked], axis=0)
        return lax.dynamic_slice_in_dim(doubled, chips - start, chips, 0)

    mine, other = natural(mine), natural(other)
    core = lane % 2
    first = jnp.where(core == 0, mine, other)
    second = jnp.where(core == 0, other, mine)
    full = jnp.stack([first, second], axis=1)
    return full.reshape((peers * array.shape[0],) + array.shape[1:]), tied


def swap_partner(array, axis):
    peers = lax.axis_size(axis)
    pairs = [(i, i ^ 1) for i in range(peers)]
    return lax.ppermute(array, axis, pairs)


def per_device(tokens, query_weight, key_weight, value_weight, chosen):
    token_rows = tokens.shape[0]
    head_width = key_weight.shape[1]
    lane_count = lax.axis_size("fsdp")
    lane_index = lax.axis_index("fsdp")
    group_index = lax.axis_index(("cy", "cx"))
    blocks_group = lane_count // 2
    my_block = group_index * blocks_group + lane_index // 2
    global_index = group_index * lane_count + lane_index

    kv_weight = lax.all_gather(
        jnp.concatenate([key_weight, value_weight], axis=1), "fsdp", axis=0, tiled=True
    )
    q_weight, kv_weight = ring_gather_rows(query_weight, "fsdp", 2, kv_weight)
    kv_f32 = jnp.dot(tokens, kv_weight, preferred_element_type=jnp.float32)
    key_value = kv_f32.astype(jnp.bfloat16)

    along_x = lax.all_gather(key_value[None], "cx", axis=0, tiled=True)
    candidates = lax.all_gather(along_x[None], "cy", axis=0, tiled=True).reshape(
        (-1,) + key_value.shape
    )
    before_pair = from_behind(key_value, ("cy", "cx", "fsdp"), 1)
    own_block = jnp.concatenate([before_pair, key_value], axis=0)

    queries = jnp.dot(tokens, q_weight, preferred_element_type=jnp.float32)
    queries = queries.astype(jnp.bfloat16).reshape(token_rows, QH, head_width)

    queries, chosen = lax.optimization_barrier((queries, chosen))

    dest_block = group_index * blocks_group + jnp.arange(lane_count, dtype=jnp.int32) // 2
    dest_pick = chosen[dest_block, jnp.arange(lane_count, dtype=jnp.int32) % 2]
    outgoing = jnp.take(candidates, dest_pick // blocks_group, axis=0, mode="clip")
    needed = dest_pick % blocks_group == lane_index // 2
    outgoing = jnp.where(needed[:, None, None], outgoing, jnp.zeros_like(outgoing))
    incoming = lax.all_to_all(outgoing, "fsdp", split_axis=0, concat_axis=0, tiled=True)

    mine = lax.dynamic_index_in_dim(chosen, my_block, 0, keepdims=False)
    my_choice = lane_index % 2
    my_pick = jnp.where(my_choice == 0, mine[0], mine[1])
    place = my_pick % blocks_group * 2
    block_mine = lax.dynamic_slice_in_dim(incoming, place, 2, 0).reshape(
        2 * token_rows, 2 * head_width
    )
    block_partner = swap_partner(block_mine, "fsdp")

    scale = head_width ** (-0.5)
    scores = jnp.concatenate(
        [
            jnp.einsum(
                "qhd,kd->hqk", queries, rows[:, :head_width], preferred_element_type=jnp.float32
            )
            for rows in (own_block, block_mine, block_partner)
        ],
        axis=2,
    ) * scale
    value_rows = jnp.concatenate(
        [own_block[:, head_width:], block_mine[:, head_width:], block_partner[:, head_width:]],
        axis=0,
    )
    window_rows = own_block.shape[0]
    pick_rows = block_mine.shape[0]
    row_index = jnp.arange(token_rows, dtype=jnp.int32)
    column = jnp.arange(window_rows, dtype=jnp.int32)
    causal = (column[None, :] <= row_index[:, None] + token_rows) & (
        (column[None, :] >= token_rows) | (global_index > 0)
    )
    first_ok = mine[0] < my_block - 1
    second_ok = (mine[1] < my_block - 1) & (mine[1] != mine[0])
    mine_ok = jnp.where(my_choice == 0, first_ok, second_ok)
    partner_ok = jnp.where(my_choice == 0, second_ok, first_ok)
    visible = jnp.concatenate(
        [
            causal,
            jnp.broadcast_to(mine_ok, (token_rows, pick_rows)),
            jnp.broadcast_to(partner_ok, (token_rows, pick_rows)),
        ],
        axis=1,
    )
    scores = jnp.where(visible[None], scores, -jnp.inf)
    highest = jnp.max(scores, axis=2, keepdims=True)
    probs = jnp.exp(scores - highest)
    denominator = jnp.sum(probs, axis=2, keepdims=True)
    mixed = (
        jnp.einsum(
            "hqk,kd->hqd",
            probs.astype(jnp.bfloat16),
            value_rows,
            preferred_element_type=jnp.float32,
        )
        / denominator
    )
    return jnp.transpose(mixed, (1, 0, 2)).reshape(token_rows, -1).astype(jnp.bfloat16)


def split_ctx(mesh):
    column = mesh.devices[:, 0]
    coords = [getattr(device, "coords", None) for device in column]
    if any(c is None for c in coords):
        across = 1
    else:
        across = len({c[0] for c in coords})
    groups, lanes = mesh.devices.shape
    return Mesh(mesh.devices.reshape(groups // across, across, lanes), ("cy", "cx", "fsdp"))


def solution(mesh):
    split = split_ctx(mesh)
    rows = P(("cy", "cx", "fsdp"), None)
    return jax.shard_map(
        per_device,
        mesh=split,
        in_specs=(rows, P("fsdp", None), P("fsdp", None), P("fsdp", None), P()),
        out_specs=rows,
        check_vma=False,
    )
```

```python
import jax
import jax.numpy as jnp
from jax import lax
from jax.experimental.layout import Layout, with_layout_constraint
from jax.sharding import Mesh, PartitionSpec as P

QH = 4


def from_behind(array, axis, by):
    peers = lax.axis_size(axis)
    pairs = [(i, i + by) for i in range(peers) if 0 <= i + by < peers]
    return lax.ppermute(array, axis, pairs)


def gather_rows(array, axis):
    peers = lax.axis_size(axis)
    spread = jnp.broadcast_to(array[None], (peers,) + array.shape)
    got = lax.all_to_all(spread, axis, split_axis=0, concat_axis=0, tiled=True)
    return got.reshape((peers * array.shape[0],) + array.shape[1:])


def ring_gather_rows(array, axis, early_steps, tied):
    peers = lax.axis_size(axis)
    chips = peers // 2
    shift_pairs = lambda by: [(i, (i + by) % peers) for i in range(peers)]
    ahead = array
    behind = array
    from_ahead = []
    from_behind_ = []
    for step in range(chips // 2):
        if step == early_steps:
            ahead, behind, tied = lax.optimization_barrier((ahead, behind, tied))
            from_ahead[-1] = ahead
            if from_behind_:
                from_behind_[-1] = behind
        ahead = lax.ppermute(ahead, axis, shift_pairs(2))
        from_ahead.append(ahead)
        if step < chips // 2 - 1:
            behind = lax.ppermute(behind, axis, shift_pairs(-2))
            from_behind_.append(behind)
    mine = jnp.stack(from_ahead[::-1] + [array] + from_behind_, axis=0)
    other = lax.ppermute(mine, axis, [(i, i ^ 1) for i in range(peers)])
    lane = lax.axis_index(axis)
    start = (lane // 2 - chips // 2) % chips

    def natural(stacked):
        doubled = jnp.concatenate([stacked, stacked], axis=0)
        return lax.dynamic_slice_in_dim(doubled, chips - start, chips, 0)

    mine, other = natural(mine), natural(other)
    core = lane % 2
    first = jnp.where(core == 0, mine, other)
    second = jnp.where(core == 0, other, mine)
    full = jnp.stack([first, second], axis=1)
    return full.reshape((peers * array.shape[0],) + array.shape[1:]), tied


def swap_partner(array, axis):
    peers = lax.axis_size(axis)
    pairs = [(i, i ^ 1) for i in range(peers)]
    return lax.ppermute(array, axis, pairs)


def per_device(tokens, query_weight, key_weight, value_weight, chosen):
    token_rows = tokens.shape[0]
    head_width = key_weight.shape[1]
    lane_count = lax.axis_size("fsdp")
    lane_index = lax.axis_index("fsdp")
    group_index = lax.axis_index(("cy", "cx"))
    blocks_group = lane_count // 2
    my_block = group_index * blocks_group + lane_index // 2
    global_index = group_index * lane_count + lane_index

    kv_weight = lax.all_gather(
        jnp.concatenate([key_weight, value_weight], axis=1), "fsdp", axis=0, tiled=True
    )
    q_weight, kv_weight = ring_gather_rows(query_weight, "fsdp", 2, kv_weight)
    kv_f32 = jnp.dot(tokens, kv_weight, preferred_element_type=jnp.float32)
    key_value = kv_f32.astype(jnp.bfloat16)

    along_x = lax.all_gather(key_value[None], "cx", axis=0, tiled=True)
    candidates = lax.all_gather(along_x[None], "cy", axis=0, tiled=True).reshape(
        (-1,) + key_value.shape
    )
    before_pair = from_behind(key_value, ("cy", "cx", "fsdp"), 1)
    own_block = jnp.concatenate([before_pair, key_value], axis=0)

    queries = jnp.dot(tokens, q_weight, preferred_element_type=jnp.float32)
    queries = queries.astype(jnp.bfloat16).reshape(token_rows, QH, head_width)

    queries, chosen = lax.optimization_barrier((queries, chosen))

    dest_block = group_index * blocks_group + jnp.arange(lane_count, dtype=jnp.int32) // 2
    dest_pick = chosen[dest_block, jnp.arange(lane_count, dtype=jnp.int32) % 2]
    outgoing = jnp.take(candidates, dest_pick // blocks_group, axis=0, mode="clip")
    outgoing = with_layout_constraint(outgoing, Layout(major_to_minor=(0, 2, 1)))
    incoming = lax.all_to_all(outgoing, "fsdp", split_axis=0, concat_axis=0, tiled=True)

    mine = lax.dynamic_index_in_dim(chosen, my_block, 0, keepdims=False)
    my_choice = lane_index % 2
    my_pick = jnp.where(my_choice == 0, mine[0], mine[1])
    place = my_pick % blocks_group * 2
    block_mine = lax.dynamic_slice_in_dim(incoming, place, 2, 0).reshape(
        2 * token_rows, 2 * head_width
    )
    block_partner = swap_partner(block_mine, "fsdp")

    scale = head_width ** (-0.5)
    scores = jnp.concatenate(
        [
            jnp.einsum(
                "qhd,kd->hqk", queries, rows[:, :head_width], preferred_element_type=jnp.float32
            )
            for rows in (own_block, block_mine, block_partner)
        ],
        axis=2,
    ) * scale
    value_rows = jnp.concatenate(
        [own_block[:, head_width:], block_mine[:, head_width:], block_partner[:, head_width:]],
        axis=0,
    )
    window_rows = own_block.shape[0]
    pick_rows = block_mine.shape[0]
    row_index = jnp.arange(token_rows, dtype=jnp.int32)
    column = jnp.arange(window_rows, dtype=jnp.int32)
    causal = (column[None, :] <= row_index[:, None] + token_rows) & (
        (column[None, :] >= token_rows) | (global_index > 0)
    )
    first_ok = mine[0] < my_block - 1
    second_ok = (mine[1] < my_block - 1) & (mine[1] != mine[0])
    mine_ok = jnp.where(my_choice == 0, first_ok, second_ok)
    partner_ok = jnp.where(my_choice == 0, second_ok, first_ok)
    visible = jnp.concatenate(
        [
            causal,
            jnp.broadcast_to(mine_ok, (token_rows, pick_rows)),
            jnp.broadcast_to(partner_ok, (token_rows, pick_rows)),
        ],
        axis=1,
    )
    scores = jnp.where(visible[None], scores, -jnp.inf)
    highest = jnp.max(scores, axis=2, keepdims=True)
    probs = jnp.exp(scores - highest)
    denominator = jnp.sum(probs, axis=2, keepdims=True)
    mixed = (
        jnp.einsum(
            "hqk,kd->hqd",
            probs.astype(jnp.bfloat16),
            value_rows,
            preferred_element_type=jnp.float32,
        )
        / denominator
    )
    return jnp.transpose(mixed, (1, 0, 2)).reshape(token_rows, -1).astype(jnp.bfloat16)


def split_ctx(mesh):
    column = mesh.devices[:, 0]
    coords = [getattr(device, "coords", None) for device in column]
    if any(c is None for c in coords):
        across = 1
    else:
        across = len({c[0] for c in coords})
    groups, lanes = mesh.devices.shape
    return Mesh(mesh.devices.reshape(groups // across, across, lanes), ("cy", "cx", "fsdp"))


def solution(mesh):
    split = split_ctx(mesh)
    rows = P(("cy", "cx", "fsdp"), None)
    return jax.shard_map(
        per_device,
        mesh=split,
        in_specs=(rows, P("fsdp", None), P("fsdp", None), P("fsdp", None), P()),
        out_specs=rows,
        check_vma=False,
    )
```

```python
import jax
import jax.numpy as jnp
from jax import lax
from jax.sharding import Mesh, PartitionSpec as P

QH = 4


def from_behind(array, axis, by):
    peers = lax.axis_size(axis)
    pairs = [(i, i + by) for i in range(peers) if 0 <= i + by < peers]
    return lax.ppermute(array, axis, pairs)


def gather_rows(array, axis):
    peers = lax.axis_size(axis)
    spread = jnp.broadcast_to(array[None], (peers,) + array.shape)
    got = lax.all_to_all(spread, axis, split_axis=0, concat_axis=0, tiled=True)
    return got.reshape((peers * array.shape[0],) + array.shape[1:])


def ring_gather_rows(array, axis, early_steps, tied):
    peers = lax.axis_size(axis)
    chips = peers // 2
    shift_pairs = lambda by: [(i, (i + by) % peers) for i in range(peers)]
    ahead = array
    behind = array
    from_ahead = []
    from_behind_ = []
    for step in range(chips // 2):
        if step == early_steps:
            ahead, behind, tied = lax.optimization_barrier((ahead, behind, tied))
            from_ahead[-1] = ahead
            if from_behind_:
                from_behind_[-1] = behind
        ahead = lax.ppermute(ahead, axis, shift_pairs(2))
        from_ahead.append(ahead)
        if step < chips // 2 - 1:
            behind = lax.ppermute(behind, axis, shift_pairs(-2))
            from_behind_.append(behind)
    mine = jnp.stack(from_ahead[::-1] + [array] + from_behind_, axis=0)
    other = lax.ppermute(mine, axis, [(i, i ^ 1) for i in range(peers)])
    lane = lax.axis_index(axis)
    start = (lane // 2 - chips // 2) % chips

    def natural(stacked):
        doubled = jnp.concatenate([stacked, stacked], axis=0)
        return lax.dynamic_slice_in_dim(doubled, chips - start, chips, 0)

    mine, other = natural(mine), natural(other)
    core = lane % 2
    first = jnp.where(core == 0, mine, other)
    second = jnp.where(core == 0, other, mine)
    full = jnp.stack([first, second], axis=1)
    return full.reshape((peers * array.shape[0],) + array.shape[1:]), tied


def swap_partner(array, axis):
    peers = lax.axis_size(axis)
    pairs = [(i, i ^ 1) for i in range(peers)]
    return lax.ppermute(array, axis, pairs)


def per_device(tokens, query_weight, key_weight, value_weight, chosen):
    token_rows = tokens.shape[0]
    head_width = key_weight.shape[1]
    lane_count = lax.axis_size("fsdp")
    lane_index = lax.axis_index("fsdp")
    group_index = lax.axis_index(("cy", "cx"))
    blocks_group = lane_count // 2
    my_block = group_index * blocks_group + lane_index // 2
    global_index = group_index * lane_count + lane_index

    kv_weight = lax.all_gather(
        jnp.concatenate([key_weight, value_weight], axis=1), "fsdp", axis=0, tiled=True
    )
    q_weight, kv_weight = ring_gather_rows(query_weight, "fsdp", 3, kv_weight)
    kv_f32 = jnp.dot(tokens, kv_weight, preferred_element_type=jnp.float32)
    key_value = kv_f32.astype(jnp.bfloat16)

    along_x = lax.all_gather(key_value[None], "cx", axis=0, tiled=True)
    candidates = lax.all_gather(along_x[None], "cy", axis=0, tiled=True).reshape(
        (-1,) + key_value.shape
    )
    before_pair = from_behind(key_value, ("cy", "cx", "fsdp"), 1)
    own_block = jnp.concatenate([before_pair, key_value], axis=0)

    queries = jnp.dot(tokens, q_weight, preferred_element_type=jnp.float32)
    queries = queries.astype(jnp.bfloat16).reshape(token_rows, QH, head_width)

    queries, chosen = lax.optimization_barrier((queries, chosen))

    dest_block = group_index * blocks_group + jnp.arange(lane_count, dtype=jnp.int32) // 2
    dest_pick = chosen[dest_block, jnp.arange(lane_count, dtype=jnp.int32) % 2]
    outgoing = jnp.take(candidates, dest_pick // blocks_group, axis=0, mode="clip")
    incoming = lax.all_to_all(outgoing, "fsdp", split_axis=0, concat_axis=0, tiled=True)

    mine = lax.dynamic_index_in_dim(chosen, my_block, 0, keepdims=False)
    my_choice = lane_index % 2
    my_pick = jnp.where(my_choice == 0, mine[0], mine[1])
    place = my_pick % blocks_group * 2
    block_mine = lax.dynamic_slice_in_dim(incoming, place, 2, 0).reshape(
        2 * token_rows, 2 * head_width
    )
    block_partner = swap_partner(block_mine, "fsdp")

    scale = head_width ** (-0.5)
    scores = jnp.concatenate(
        [
            jnp.einsum(
                "qhd,kd->hqk", queries, rows[:, :head_width], preferred_element_type=jnp.float32
            )
            for rows in (own_block, block_mine, block_partner)
        ],
        axis=2,
    ) * scale
    value_rows = jnp.concatenate(
        [own_block[:, head_width:], block_mine[:, head_width:], block_partner[:, head_width:]],
        axis=0,
    )
    window_rows = own_block.shape[0]
    pick_rows = block_mine.shape[0]
    row_index = jnp.arange(token_rows, dtype=jnp.int32)
    column = jnp.arange(window_rows, dtype=jnp.int32)
    causal = (column[None, :] <= row_index[:, None] + token_rows) & (
        (column[None, :] >= token_rows) | (global_index > 0)
    )
    first_ok = mine[0] < my_block - 1
    second_ok = (mine[1] < my_block - 1) & (mine[1] != mine[0])
    mine_ok = jnp.where(my_choice == 0, first_ok, second_ok)
    partner_ok = jnp.where(my_choice == 0, second_ok, first_ok)
    visible = jnp.concatenate(
        [
            causal,
            jnp.broadcast_to(mine_ok, (token_rows, pick_rows)),
            jnp.broadcast_to(partner_ok, (token_rows, pick_rows)),
        ],
        axis=1,
    )
    scores = jnp.where(visible[None], scores, -jnp.inf)
    highest = jnp.max(scores, axis=2, keepdims=True)
    probs = jnp.exp(scores - highest)
    denominator = jnp.sum(probs, axis=2, keepdims=True)
    mixed = (
        jnp.einsum(
            "hqk,kd->hqd",
            probs.astype(jnp.bfloat16),
            value_rows,
            preferred_element_type=jnp.float32,
        )
        / denominator
    )
    return jnp.transpose(mixed, (1, 0, 2)).reshape(token_rows, -1).astype(jnp.bfloat16)


def split_ctx(mesh):
    column = mesh.devices[:, 0]
    coords = [getattr(device, "coords", None) for device in column]
    if any(c is None for c in coords):
        across = 1
    else:
        across = len({c[0] for c in coords})
    groups, lanes = mesh.devices.shape
    return Mesh(mesh.devices.reshape(groups // across, across, lanes), ("cy", "cx", "fsdp"))


def solution(mesh):
    split = split_ctx(mesh)
    rows = P(("cy", "cx", "fsdp"), None)
    return jax.shard_map(
        per_device,
        mesh=split,
        in_specs=(rows, P("fsdp", None), P("fsdp", None), P("fsdp", None), P()),
        out_specs=rows,
        check_vma=False,
    )
```
